32 devices in a mesh: dp: 8 (over z, core), rot: 4 (over y, x).
Axes of the slice: x: 2, y: 2, z: 4, core: 2. Of those that a mesh axis runs over, the one named last changes fastest.
Arguments:
- vectors: bfloat16 [2048, 4096], P('dp', 'rot'), may hold values from -100 to 100
- rotation: bfloat16 [4096, 4096], P('rot'), may hold values from -0.125 to 0.125
- codes: int32 [2048, 256], P('dp', 'rot'), may hold values from 0 to 255
Outputs:
- codebook: float32 [4096, 256], P('rot')
- new_rotation: bfloat16 [4096, 4096], P('rot', 'dp')
The draws below stay inside these ranges and needn't reach their ends.
All inputs are finite; a program needn't handle non-finite values.
Results may differ from the reference program's by a relative error of at most 0.007.
Values may be sent and summed in bfloat16 or wider, within the bound.
No kernel may reach another device: no remote copies, remote signals or barrier semaphores. Data moves between devices by JAX's collectives and lax.ppermute only.
A program may use at most 64 MiB of HBM per device.

```python
import math
import jax
import jax.numpy as jnp
import numpy as np
from jax import lax

D = 4096
SUB = 16
K = 256
ITERS = 2
M = 256
ROWS = 2048


def draw_vectors(key, part):
    random_key_seed = jax.random.fold_in(key, 11)
    key_cols = jax.random.fold_in(key, 12)
    key_rows = jax.random.fold_in(key, 13)
    key_common = jax.random.fold_in(key, 14)
    base = jnp.clip(jax.random.normal(random_key_seed, (ROWS, D), jnp.float32), -5.0, 5.0)
    column_scale = jnp.exp(jax.random.uniform(key_cols, (1, D), jnp.float32, minval=0.0, maxval=math.log(10.0)))
    row_scale_factor = jnp.exp(jax.random.uniform(key_rows, (ROWS, 1), jnp.float32, minval=0.0, maxval=math.log(10.0)))
    common_direction = jnp.clip(jax.random.normal(key_common, (1, D), jnp.float32), -4.0, 4.0) * column_scale
    common_part = 0.29 / math.sqrt(ROWS) * row_scale_factor * common_direction
    total = 0.2 * base * column_scale * row_scale_factor + common_part
    return jnp.clip(total, -100.0, 100.0).astype(jnp.bfloat16)


def plant(drawn, rng, least, top_value):
    index_at = [jax.random.randint(jax.random.fold_in(rng, axis), (), 0, length) for axis, length in enumerate(drawn.shape)]
    widest = drawn.shape.index(max(drawn.shape))
    neighbour = index_at[:widest] + [(index_at[widest] + 1) % drawn.shape[widest]] + index_at[widest + 1:]
    return drawn.at[tuple(index_at)].set(least).at[tuple(neighbour)].set(top_value)


def spiked(array, rng, source, target, blocks, factor):
    def block_of(dim):
        return (jnp.arange(array.shape[dim]) // (array.shape[dim] // blocks)).reshape((-1,) + (1,) * (array.ndim - 1 - dim))

    one_side = jax.random.permutation(rng, blocks)[block_of(target)]
    other_side = (block_of(target) + blocks // 2) % blocks
    return jnp.where((block_of(source) == one_side) | (block_of(source) == other_side), factor * array, array)


def steps_of(stream_key, extent, split, smallest, high):
    gain, own = 1.0, jax.random.fold_in(stream_key, 6)
    for dim, parts in split:
        draws = jnp.exp(jax.random.uniform(jax.random.fold_in(own, dim), (parts,), jnp.float32, smallest / len(split), high / len(split)))
        gain = gain * jnp.repeat(draws, extent[dim] // parts).reshape([-1 if axis == dim else 1 for axis in range(len(extent))])
    return gain


def cumulative_ranks(amount, skew):
    weights = [(1 << 20) // math.isqrt(standing ** skew) + 1 for standing in range(1, amount + 1)]
    scale = 1 + sum(weights) // (1 << 30)
    return np.cumsum(np.array([max(1, weight // scale) for weight in weights]))


def skewed_ids(own_key, extent, number_of, skew):
    grid = cumulative_ranks(number_of, skew)
    ticket = jax.random.randint(jax.random.fold_in(own_key, 1), extent, 0, int(grid[number_of - 1]))
    rank = jnp.searchsorted(jnp.asarray(grid, jnp.int32), ticket, side="right")
    return jax.random.permutation(jax.random.fold_in(own_key, 2), number_of)[rank].astype(jnp.int32)


def noise_with(key, shape, spread, reach, cuts, heavy, kind=jnp.bfloat16):
    result = spread * jax.random.normal(key, shape, jnp.float32)
    if cuts:
        result = result * steps_of(key, shape, cuts, -0.22, 0.18)
    return jnp.clip(spiked(result, jax.random.fold_in(key, 3), *heavy), -reach, reach).astype(kind)


def setup_inputs(seed: int = 0) -> dict:
    splits = jax.random.split(jax.random.key(seed), 4)
    return {
        "vectors": draw_vectors(jax.random.fold_in(splits[3], 71), 0),
        "rotation": noise_with(splits[1], (D, D), D ** -0.5, 0.125, ((0, 4),), (0, 1, 4, 2.0)),
        "codes": plant(skewed_ids(splits[2], (ROWS, M), K, 2), jax.random.fold_in(splits[2], 3), 0, K - 1).astype(jnp.int32),
    }


def subspace_totals(args):
    rot_part, code_part = args
    code_indicator = (code_part[:, None] == jnp.arange(K, dtype=jnp.int32)[None, :]).astype(jnp.bfloat16)
    sums = lax.dot_general(rot_part, code_indicator, (((0,), (0,)), ((), ())), preferred_element_type=jnp.float32)
    counts = lax.optimization_barrier(jnp.sum(code_indicator.astype(jnp.float32), axis=0))
    return (sums, counts)

def reference(vectors, rotation, codes):
    rotated = jnp.dot(vectors, rotation, preferred_element_type=jnp.float32).astype(jnp.bfloat16)
    grouped_vectors = rotated.reshape(ROWS, M, SUB).transpose(1, 0, 2)
    codes_t = codes.T
    sums, counts = lax.map(subspace_totals, (grouped_vectors, codes_t))
    book = sums / jnp.maximum(counts, 1.0)[:, None, :]
    codebook = book.reshape(D, K)
    codebook_batch = book.astype(jnp.bfloat16)

    def reconstruct(args):
        entries, code_part = args
        return jnp.take(entries, code_part, axis=1)
    reconstructed_transposed = lax.map(reconstruct, (codebook_batch, codes_t)).reshape(D, ROWS)
    cross = lax.dot_general(vectors, reconstructed_transposed, (((0,), (1,)), ((), ())), preferred_element_type=jnp.float32)
    cross_b = cross.astype(jnp.bfloat16)
    raw = lax.dot_general(cross_b, cross_b, (((0,), (0,)), ((), ())), preferred_element_type=jnp.float32)
    scale = 1.7 / jnp.sqrt(jnp.sqrt(jnp.sum(raw * raw)))
    gram_b = (scale * scale * raw).astype(jnp.bfloat16)
    product = jnp.dot(cross_b, gram_b, preferred_element_type=jnp.float32)
    iterate = scale * (1.5 * cross_b.astype(jnp.float32) - 0.5 * product)
    for iteration in range(ITERS - 1):
        rows_b = iterate.astype(jnp.bfloat16)
        gram = lax.dot_general(rows_b, rows_b, (((0,), (0,)), ((), ())), preferred_element_type=jnp.float32)
        gram_b = gram.astype(jnp.bfloat16)
        product = jnp.dot(rows_b, gram_b, preferred_element_type=jnp.float32)
        iterate = 1.5 * rows_b.astype(jnp.float32) - 0.5 * product
    new_rotation = (math.sqrt(D) * iterate).astype(jnp.bfloat16)
    return (codebook, new_rotation)
```

```python
import math

import jax
import jax.numpy as jnp
from jax import lax
from jax.sharding import PartitionSpec as P

K = 256
ITERS = 2


def body(vectors, rotation, codes):
    row_count, block_dims = vectors.shape
    width = rotation.shape[1]
    local_spaces = codes.shape[1]
    sub_dims = block_dims // local_spaces
    tile_cols = width // lax.axis_size("dp")
    tile_spaces = tile_cols // sub_dims
    dp_index = lax.axis_index("dp")
    code_ids = jnp.arange(K, dtype=jnp.int32)

    all_vectors = lax.all_gather(vectors, "dp", axis=0, tiled=True)
    all_codes = lax.all_gather(
        lax.all_gather(codes, "rot", axis=1, tiled=True), "dp", axis=0, tiled=True
    )
    tile_codes = lax.dynamic_slice_in_dim(all_codes, dp_index * tile_spaces, tile_spaces, 1)

    rotated_t = lax.psum_scatter(
        lax.dot_general(
            rotation, vectors, (((0,), (1,)), ((), ())), preferred_element_type=jnp.float32
        ),
        "rot",
        scatter_dimension=0,
        tiled=True,
    ).astype(jnp.bfloat16)
    code_indicator = (codes.T[:, :, None] == code_ids[None, None, :]).astype(jnp.bfloat16)
    grouped_vectors = rotated_t.reshape(local_spaces, sub_dims, row_count)
    shard_code_sums = jnp.einsum(
        "vzo,voc->vzc", grouped_vectors, code_indicator, preferred_element_type=jnp.float32
    )
    local_counts = jnp.sum(code_indicator, axis=1, dtype=jnp.float32)
    total_sums, total_counts = lax.psum((shard_code_sums, local_counts), "dp")
    book = total_sums / jnp.maximum(total_counts, 1.0)[:, None, :]
    codebook = book.reshape(block_dims, K)
    codebook_batch = lax.all_gather(book.astype(jnp.bfloat16), "rot", axis=0, tiled=True)
    tile_book = lax.dynamic_slice_in_dim(codebook_batch, dp_index * tile_spaces, tile_spaces, 0)

    tile_indicator = (tile_codes.T[:, :, None] == code_ids[None, None, :]).astype(jnp.bfloat16)
    rebuilt_t = jnp.einsum(
        "lyg,lxg->lyx", tile_book, tile_indicator, preferred_element_type=jnp.float32
    )
    rebuilt_t = rebuilt_t.astype(jnp.bfloat16).reshape(tile_cols, all_vectors.shape[0])
    cross_tile = lax.dot_general(
        all_vectors, rebuilt_t, (((0,), (1,)), ((), ())), preferred_element_type=jnp.float32
    ).astype(jnp.bfloat16)

    def apply_gram(rows_b, gram_b):
        return jnp.dot(
            rows_b,
            lax.all_gather(gram_b, "rot", axis=0, tiled=True),
            preferred_element_type=jnp.float32,
        )

    columns = cross_tile
    new_tile = None
    for iteration in range(ITERS):
        rows_b = lax.all_gather(columns, "dp", axis=1, tiled=True)
        gram_part = lax.psum_scatter(
            lax.dot_general(
                rows_b,
                columns,
                (((0,), (0,)), ((), ())),
                preferred_element_type=jnp.float32,
            ),
            "rot",
            scatter_dimension=0,
            tiled=True,
        )
        if iteration == 0:
            total = lax.psum(jnp.sum(gram_part * gram_part), ("dp", "rot"))
            factor = 1.7 / jnp.sqrt(jnp.sqrt(total))
            gram_b = (factor * factor * gram_part).astype(jnp.bfloat16)
            product = apply_gram(rows_b, gram_b)
            new_tile = factor * (1.5 * columns.astype(jnp.float32) - 0.5 * product)
        else:
            gram_b = gram_part.astype(jnp.bfloat16)
            product = apply_gram(rows_b, gram_b)
            new_tile = 1.5 * columns.astype(jnp.float32) - 0.5 * product
        columns = new_tile.astype(jnp.bfloat16)
    new_rotation = (math.sqrt(width) * new_tile).astype(jnp.bfloat16)
    return (codebook, new_rotation)


def solution(mesh):
    return jax.shard_map(
        body,
        mesh=mesh,
        in_specs=(P("dp", "rot"), P("rot", None), P("dp", "rot")),
        out_specs=(P("rot", None), P("rot", "dp")),
        check_vma=False,
    )
```

```python
import math

import jax
import jax.numpy as jnp
from jax import lax
from jax.sharding import PartitionSpec as P

K = 256
ITERS = 2


def body(vectors, rotation, codes):
    row_count, block_dims = vectors.shape
    width = rotation.shape[1]
    local_spaces = codes.shape[1]
    sub_dims = block_dims // local_spaces
    tile_cols = width // lax.axis_size("dp")
    tile_spaces = tile_cols // sub_dims
    dp_index = lax.axis_index("dp")
    code_ids = jnp.arange(K, dtype=jnp.int32)

    dp_size = lax.axis_size("dp")
    row_codes = lax.all_gather(codes, "rot", axis=1, tiled=True)
    vector_parts = [vectors]
    code_parts = [lax.dynamic_slice_in_dim(row_codes, dp_index * tile_spaces, tile_spaces, 1)]
    for shift in range(1, dp_size):
        pairs = [(i, (i + shift) % dp_size) for i in range(dp_size)]
        target = (dp_index + shift) % dp_size
        vector_parts.append(lax.ppermute(vectors, "dp", pairs))
        code_parts.append(
            lax.ppermute(
                lax.dynamic_slice_in_dim(row_codes, target * tile_spaces, tile_spaces, 1),
                "dp",
                pairs,
            )
        )
    all_vectors = jnp.concatenate(vector_parts, axis=0)
    tile_codes = jnp.concatenate(code_parts, axis=0)

    rotated_t = lax.psum_scatter(
        lax.dot_general(
            rotation, vectors, (((0,), (1,)), ((), ())), preferred_element_type=jnp.float32
        ),
        "rot",
        scatter_dimension=0,
        tiled=True,
    ).astype(jnp.bfloat16)
    code_indicator = (codes.T[:, :, None] == code_ids[None, None, :]).astype(jnp.bfloat16)
    grouped_vectors = rotated_t.reshape(local_spaces, sub_dims, row_count)
    shard_code_sums = jnp.einsum(
        "vzo,voc->vzc", grouped_vectors, code_indicator, preferred_element_type=jnp.float32
    )
    local_counts = jnp.sum(code_indicator, axis=1, dtype=jnp.float32)
    total_sums, total_counts = lax.psum((shard_code_sums, local_counts), "dp")
    book = total_sums / jnp.maximum(total_counts, 1.0)[:, None, :]
    codebook = book.reshape(block_dims, K)
    codebook_batch = lax.all_gather(book.astype(jnp.bfloat16), "rot", axis=0, tiled=True)
    tile_book = lax.dynamic_slice_in_dim(codebook_batch, dp_index * tile_spaces, tile_spaces, 0)

    tile_indicator = (tile_codes.T[:, :, None] == code_ids[None, None, :]).astype(jnp.bfloat16)
    rebuilt_t = jnp.einsum(
        "lyg,lxg->lyx", tile_book, tile_indicator, preferred_element_type=jnp.float32
    )
    rebuilt_t = rebuilt_t.astype(jnp.bfloat16).reshape(tile_cols, all_vectors.shape[0])
    cross_tile = lax.dot_general(
        all_vectors, rebuilt_t, (((0,), (1,)), ((), ())), preferred_element_type=jnp.float32
    ).astype(jnp.bfloat16)

    def apply_gram(rows_b, gram_b):
        return jnp.dot(
            rows_b,
            lax.all_gather(gram_b, "rot", axis=0, tiled=True),
            preferred_element_type=jnp.float32,
        )

    columns = cross_tile
    new_tile = None
    for iteration in range(ITERS):
        rows_b = lax.all_gather(columns, "dp", axis=1, tiled=True)
        gram_part = lax.psum_scatter(
            lax.dot_general(
                rows_b,
                columns,
                (((0,), (0,)), ((), ())),
                preferred_element_type=jnp.float32,
            ),
            "rot",
            scatter_dimension=0,
            tiled=True,
        )
        if iteration == 0:
            total = lax.psum(jnp.sum(gram_part * gram_part), ("dp", "rot"))
            factor = 1.7 / jnp.sqrt(jnp.sqrt(total))
            product = apply_gram(rows_b, gram_part.astype(jnp.bfloat16))
            new_tile = factor * (
                1.5 * columns.astype(jnp.float32) - 0.5 * (factor * factor) * product
            )
        else:
            gram_b = gram_part.astype(jnp.bfloat16)
            product = apply_gram(rows_b, gram_b)
            new_tile = 1.5 * columns.astype(jnp.float32) - 0.5 * product
        columns = new_tile.astype(jnp.bfloat16)
    new_rotation = (math.sqrt(width) * new_tile).astype(jnp.bfloat16)
    return (codebook, new_rotation)


def solution(mesh):
    return jax.shard_map(
        body,
        mesh=mesh,
        in_specs=(P("dp", "rot"), P("rot", None), P("dp", "rot")),
        out_specs=(P("rot", None), P("rot", "dp")),
        check_vma=False,
    )
```

```python
import math

import jax
import jax.numpy as jnp
from jax import lax
from jax.sharding import PartitionSpec as P

K = 256
ITERS = 2


def body(vectors, rotation, codes):
    row_count, block_dims = vectors.shape
    width = rotation.shape[1]
    local_spaces = codes.shape[1]
    sub_dims = block_dims // local_spaces
    tile_cols = width // lax.axis_size("dp")
    tile_spaces = tile_cols // sub_dims
    dp_index = lax.axis_index("dp")
    code_ids = jnp.arange(K, dtype=jnp.int32)

    dp_size = lax.axis_size("dp")
    row_codes = lax.all_gather(codes, "rot", axis=1, tiled=True)
    vector_parts = [vectors]
    code_parts = [lax.dynamic_slice_in_dim(row_codes, dp_index * tile_spaces, tile_spaces, 1)]
    for shift in range(1, dp_size):
        pairs = [(i, (i + shift) % dp_size) for i in range(dp_size)]
        target = (dp_index + shift) % dp_size
        vector_parts.append(lax.ppermute(vectors, "dp", pairs))
        code_parts.append(
            lax.ppermute(
                lax.dynamic_slice_in_dim(row_codes, target * tile_spaces, tile_spaces, 1),
                "dp",
                pairs,
            )
        )
    all_vectors = jnp.concatenate(vector_parts, axis=0)
    tile_codes = jnp.concatenate(code_parts, axis=0)

    rotated_t = lax.psum_scatter(
        lax.dot_general(
            rotation, vectors, (((0,), (1,)), ((), ())), preferred_element_type=jnp.float32
        ),
        "rot",
        scatter_dimension=0,
        tiled=True,
    ).astype(jnp.bfloat16)
    rotated_t, all_vectors, tile_codes = lax.optimization_barrier(
        (rotated_t, all_vectors, tile_codes)
    )
    code_indicator = (codes.T[:, :, None] == code_ids[None, None, :]).astype(jnp.bfloat16)
    grouped_vectors = rotated_t.reshape(local_spaces, sub_dims, row_count)
    shard_code_sums = jnp.einsum(
        "vzo,voc->vzc", grouped_vectors, code_indicator, preferred_element_type=jnp.float32
    )
    local_counts = jnp.sum(code_indicator, axis=1, dtype=jnp.float32)
    total_sums, total_counts = lax.psum((shard_code_sums, local_counts), "dp")
    book = total_sums / jnp.maximum(total_counts, 1.0)[:, None, :]
    codebook = book.reshape(block_dims, K)
    codebook_batch = lax.all_gather(book.astype(jnp.bfloat16), "rot", axis=0, tiled=True)
    tile_book = lax.dynamic_slice_in_dim(codebook_batch, dp_index * tile_spaces, tile_spaces, 0)

    tile_indicator = (tile_codes.T[:, :, None] == code_ids[None, None, :]).astype(jnp.bfloat16)
    rebuilt_t = jnp.einsum(
        "lyg,lxg->lyx", tile_book, tile_indicator, preferred_element_type=jnp.float32
    )
    rebuilt_t = rebuilt_t.astype(jnp.bfloat16).reshape(tile_cols, all_vectors.shape[0])
    cross_tile = lax.dot_general(
        all_vectors, rebuilt_t, (((0,), (1,)), ((), ())), preferred_element_type=jnp.float32
    ).astype(jnp.bfloat16)

    def apply_gram(rows_b, gram_b):
        return jnp.dot(
            rows_b,
            lax.all_gather(gram_b, "rot", axis=0, tiled=True),
            preferred_element_type=jnp.float32,
        )

    columns = cross_tile
    new_tile = None
    for iteration in range(ITERS):
        rows_b = lax.all_gather(columns, "dp", axis=1, tiled=True)
        gram_part = lax.psum_scatter(
            lax.dot_general(
                rows_b,
                columns,
                (((0,), (0,)), ((), ())),
                preferred_element_type=jnp.float32,
            ),
            "rot",
            scatter_dimension=0,
            tiled=True,
        )
        if iteration == 0:
            total = lax.psum(jnp.sum(gram_part * gram_part), ("dp", "rot"))
            factor = 1.7 / jnp.sqrt(jnp.sqrt(total))
            product = apply_gram(rows_b, gram_part.astype(jnp.bfloat16))
            new_tile = factor * (
                1.5 * columns.astype(jnp.float32) - 0.5 * (factor * factor) * product
            )
        else:
            gram_b = gram_part.astype(jnp.bfloat16)
            product = apply_gram(rows_b, gram_b)
            new_tile = 1.5 * columns.astype(jnp.float32) - 0.5 * product
        columns = new_tile.astype(jnp.bfloat16)
    new_rotation = (math.sqrt(width) * new_tile).astype(jnp.bfloat16)
    return (codebook, new_rotation)


def solution(mesh):
    return jax.shard_map(
        body,
        mesh=mesh,
        in_specs=(P("dp", "rot"), P("rot", None), P("dp", "rot")),
        out_specs=(P("rot", None), P("rot", "dp")),
        check_vma=False,
    )
```

```python
import math

import jax
import jax.numpy as jnp
from jax import lax
from jax.sharding import PartitionSpec as P

K = 256
ITERS = 2


def body(vectors, rotation, codes):
    row_count, block_dims = vectors.shape
    width = rotation.shape[1]
    local_spaces = codes.shape[1]
    sub_dims = block_dims // local_spaces
    tile_cols = width // lax.axis_size("dp")
    tile_spaces = tile_cols // sub_dims
    dp_index = lax.axis_index("dp")
    code_ids = jnp.arange(K, dtype=jnp.int32)

    dp_size = lax.axis_size("dp")
    row_codes = lax.all_gather(codes, "rot", axis=1, tiled=True)

    def tile_part(block):
        block_codes = lax.dynamic_slice_in_dim(row_codes, block * tile_spaces, tile_spaces, 1)
        return jnp.concatenate([vectors, block_codes.astype(jnp.bfloat16)], axis=1)

    parts = [tile_part(dp_index)]
    for shift in range(1, dp_size):
        pairs = [(i, (i + shift) % dp_size) for i in range(dp_size)]
        parts.append(lax.ppermute(tile_part((dp_index + shift) % dp_size), "dp", pairs))
    joined = jnp.concatenate(parts, axis=0)
    all_vectors = joined[:, :block_dims]
    tile_codes = joined[:, block_dims:].astype(jnp.int32)

    rotated_t = lax.psum_scatter(
        lax.dot_general(
            rotation, vectors, (((0,), (1,)), ((), ())), preferred_element_type=jnp.float32
        ),
        "rot",
        scatter_dimension=0,
        tiled=True,
    ).astype(jnp.bfloat16)
    code_indicator = (codes.T[:, :, None] == code_ids[None, None, :]).astype(jnp.bfloat16)
    grouped_vectors = rotated_t.reshape(local_spaces, sub_dims, row_count)
    shard_code_sums = jnp.einsum(
        "vzo,voc->vzc", grouped_vectors, code_indicator, preferred_element_type=jnp.float32
    )
    local_counts = jnp.sum(code_indicator, axis=1, dtype=jnp.float32)
    total_sums, total_counts = lax.psum((shard_code_sums, local_counts), "dp")
    total_sums, total_counts, all_vectors, tile_codes = lax.optimization_barrier(
        (total_sums, total_counts, all_vectors, tile_codes)
    )
    book = total_sums / jnp.maximum(total_counts, 1.0)[:, None, :]
    codebook = book.reshape(block_dims, K)
    codebook_batch = lax.all_gather(book.astype(jnp.bfloat16), "rot", axis=0, tiled=True)
    tile_book = lax.dynamic_slice_in_dim(codebook_batch, dp_index * tile_spaces, tile_spaces, 0)

    tile_indicator = (tile_codes.T[:, :, None] == code_ids[None, None, :]).astype(jnp.bfloat16)
    rebuilt_t = jnp.einsum(
        "lyg,lxg->lyx", tile_book, tile_indicator, preferred_element_type=jnp.float32
    )
    rebuilt_t = rebuilt_t.astype(jnp.bfloat16).reshape(tile_cols, all_vectors.shape[0])
    cross_tile = lax.dot_general(
        all_vectors, rebuilt_t, (((0,), (1,)), ((), ())), preferred_element_type=jnp.float32
    ).astype(jnp.bfloat16)

    def apply_gram(rows_b, gram_b):
        return jnp.dot(
            rows_b,
            lax.all_gather(gram_b, "rot", axis=0, tiled=True),
            preferred_element_type=jnp.float32,
        )

    columns = cross_tile
    new_tile = None
    for iteration in range(ITERS):
        rows_b = lax.all_gather(columns, "dp", axis=1, tiled=True)
        gram_part = lax.psum_scatter(
            lax.dot_general(
                rows_b,
                columns,
                (((0,), (0,)), ((), ())),
                preferred_element_type=jnp.float32,
            ),
            "rot",
            scatter_dimension=0,
            tiled=True,
        )
        if iteration == 0:
            total = lax.psum(jnp.sum(gram_part * gram_part), ("dp", "rot"))
            factor = 1.7 / jnp.sqrt(jnp.sqrt(total))
            product = apply_gram(rows_b, gram_part.astype(jnp.bfloat16))
            new_tile = factor * (
                1.5 * columns.astype(jnp.float32) - 0.5 * (factor * factor) * product
            )
        else:
            gram_b = gram_part.astype(jnp.bfloat16)
            product = apply_gram(rows_b, gram_b)
            new_tile = 1.5 * columns.astype(jnp.float32) - 0.5 * product
        columns = new_tile.astype(jnp.bfloat16)
    new_rotation = (math.sqrt(width) * new_tile).astype(jnp.bfloat16)
    return (codebook, new_rotation)


def solution(mesh):
    return jax.shard_map(
        body,
        mesh=mesh,
        in_specs=(P("dp", "rot"), P("rot", None), P("dp", "rot")),
        out_specs=(P("rot", None), P("rot", "dp")),
        check_vma=False,
    )
```

```python
import math

import jax
import jax.numpy as jnp
from jax import lax
from jax.sharding import PartitionSpec as P

K = 256
ITERS = 2


def body(vectors, rotation, codes):
    row_count, block_dims = vectors.shape
    width = rotation.shape[1]
    local_spaces = codes.shape[1]
    sub_dims = block_dims // local_spaces
    tile_cols = width // lax.axis_size("dp")
    tile_spaces = tile_cols // sub_dims
    dp_index = lax.axis_index("dp")
    code_ids = jnp.arange(K, dtype=jnp.int32)

    dp_size = lax.axis_size("dp")
    row_codes = lax.all_gather(codes, "rot", axis=1, tiled=True)

    def tile_part(block):
        block_codes = lax.dynamic_slice_in_dim(row_codes, block * tile_spaces, tile_spaces, 1)
        return jnp.concatenate([vectors, block_codes.astype(jnp.bfloat16)], axis=1)

    parts = [tile_part(dp_index)]
    for shift in range(1, dp_size):
        pairs = [(i, (i + shift) % dp_size) for i in range(dp_size)]
        parts.append(lax.ppermute(tile_part((dp_index + shift) % dp_size), "dp", pairs))
    joined = jnp.concatenate(parts, axis=0)
    all_vectors = joined[:, :block_dims]
    tile_codes = joined[:, block_dims:].astype(jnp.int32)

    rotated_t = lax.psum_scatter(
        lax.dot_general(
            rotation, vectors, (((0,), (1,)), ((), ())), preferred_element_type=jnp.float32
        ),
        "rot",
        scatter_dimension=0,
        tiled=True,
    ).astype(jnp.bfloat16)
    code_indicator = (codes.T[:, :, None] == code_ids[None, None, :]).astype(jnp.bfloat16)
    grouped_vectors = rotated_t.reshape(local_spaces, sub_dims, row_count)
    shard_code_sums = jnp.einsum(
        "vzo,voc->vzc", grouped_vectors, code_indicator, preferred_element_type=jnp.float32
    )
    local_counts = jnp.sum(code_indicator, axis=1, dtype=jnp.float32)
    total_sums, total_counts = lax.psum((shard_code_sums, local_counts), "dp")
    total_sums, total_counts, all_vectors, tile_codes = lax.optimization_barrier(
        (total_sums, total_counts, all_vectors, tile_codes)
    )
    book = total_sums / jnp.maximum(total_counts, 1.0)[:, None, :]
    codebook = book.reshape(block_dims, K)
    codebook_batch = lax.all_gather(book.astype(jnp.bfloat16), "rot", axis=0, tiled=True)
    tile_book = lax.dynamic_slice_in_dim(codebook_batch, dp_index * tile_spaces, tile_spaces, 0)

    tile_indicator = (tile_codes.T[:, :, None] == code_ids[None, None, :]).astype(jnp.bfloat16)
    rebuilt_t = jnp.einsum(
        "lyg,lxg->lyx", tile_book, tile_indicator, preferred_element_type=jnp.float32
    )
    rebuilt_t = rebuilt_t.astype(jnp.bfloat16).reshape(tile_cols, all_vectors.shape[0])
    cross_tile = lax.dot_general(
        all_vectors, rebuilt_t, (((0,), (1,)), ((), ())), preferred_element_type=jnp.float32
    ).astype(jnp.bfloat16)

    def gram_step(tile, first):
        parts = [tile]
        for shift in range(1, dp_size):
            pairs = [(i, (i + shift) % dp_size) for i in range(dp_size)]
            parts.append(lax.ppermute(tile, "dp", pairs))
        half = dp_size // 2
        panels = [jnp.concatenate(parts[:half], axis=1), jnp.concatenate(parts[half:], axis=1)]
        pieces = [
            lax.psum_scatter(
                lax.dot_general(
                    panel, tile, (((0,), (0,)), ((), ())), preferred_element_type=jnp.float32
                ),
                "rot",
                scatter_dimension=0,
                tiled=True,
            )
            for panel in panels
        ]
        product = None
        for panel, piece in zip(panels, pieces):
            gathered = lax.all_gather(piece.astype(jnp.bfloat16), "rot", axis=0, tiled=True)
            term = jnp.dot(panel, gathered, preferred_element_type=jnp.float32)
            product = term if product is None else product + term
        if first:
            squares = sum(jnp.sum(piece * piece) for piece in pieces)
            factor = 1.7 / jnp.sqrt(jnp.sqrt(lax.psum(squares, ("dp", "rot"))))
            return factor * (1.5 * tile.astype(jnp.float32) - 0.5 * (factor * factor) * product)
        return 1.5 * tile.astype(jnp.float32) - 0.5 * product

    new_tile = None
    columns = cross_tile
    for iteration in range(ITERS):
        new_tile = gram_step(columns, iteration == 0)
        columns = new_tile.astype(jnp.bfloat16)
    new_rotation = (math.sqrt(width) * new_tile).astype(jnp.bfloat16)
    return (codebook, new_rotation)


def solution(mesh):
    return jax.shard_map(
        body,
        mesh=mesh,
        in_specs=(P("dp", "rot"), P("rot", None), P("dp", "rot")),
        out_specs=(P("rot", None), P("rot", "dp")),
        check_vma=False,
    )
```

```python
import math

import jax
import jax.numpy as jnp
from jax import lax
from jax.sharding import PartitionSpec as P

K = 256
ITERS = 2


def body(vectors, rotation, codes):
    row_count, block_dims = vectors.shape
    width = rotation.shape[1]
    local_spaces = codes.shape[1]
    sub_dims = block_dims // local_spaces
    tile_cols = width // lax.axis_size("dp")
    tile_spaces = tile_cols // sub_dims
    dp_index = lax.axis_index("dp")
    code_ids = jnp.arange(K, dtype=jnp.int32)

    dp_size = lax.axis_size("dp")
    row_codes = lax.all_gather(codes, "rot", axis=1, tiled=True)

    def tile_part(block):
        block_codes = lax.dynamic_slice_in_dim(row_codes, block * tile_spaces, tile_spaces, 1)
        return jnp.concatenate([vectors, block_codes.astype(jnp.bfloat16)], axis=1)

    parts = [tile_part(dp_index)]
    for shift in range(1, dp_size):
        pairs = [(i, (i + shift) % dp_size) for i in range(dp_size)]
        parts.append(lax.ppermute(tile_part((dp_index + shift) % dp_size), "dp", pairs))
    joined = jnp.concatenate(parts, axis=0)
    all_vectors = joined[:, :block_dims]
    tile_codes = joined[:, block_dims:].astype(jnp.int32)

    rotated_t = lax.psum_scatter(
        lax.dot_general(
            rotation, vectors, (((0,), (1,)), ((), ())), preferred_element_type=jnp.float32
        ),
        "rot",
        scatter_dimension=0,
        tiled=True,
    ).astype(jnp.bfloat16)
    code_indicator = (codes.T[:, :, None] == code_ids[None, None, :]).astype(jnp.bfloat16)
    grouped_vectors = rotated_t.reshape(local_spaces, sub_dims, row_count)
    shard_code_sums = jnp.einsum(
        "vzo,voc->vzc", grouped_vectors, code_indicator, preferred_element_type=jnp.float32
    )
    local_counts = jnp.sum(code_indicator, axis=1, dtype=jnp.float32)
    total_sums, total_counts = lax.psum((shard_code_sums, local_counts), "dp")
    total_sums, total_counts, all_vectors, tile_codes = lax.optimization_barrier(
        (total_sums, total_counts, all_vectors, tile_codes)
    )
    book = total_sums / jnp.maximum(total_counts, 1.0)[:, None, :]
    codebook = book.reshape(block_dims, K)
    codebook_batch = lax.all_gather(book.astype(jnp.bfloat16), "rot", axis=0, tiled=True)
    tile_book = lax.dynamic_slice_in_dim(codebook_batch, dp_index * tile_spaces, tile_spaces, 0)

    tile_indicator = (tile_codes.T[:, :, None] == code_ids[None, None, :]).astype(jnp.bfloat16)
    rebuilt_t = jnp.einsum(
        "lyg,lxg->lyx", tile_book, tile_indicator, preferred_element_type=jnp.float32
    )
    rebuilt_t = rebuilt_t.astype(jnp.bfloat16).reshape(tile_cols, all_vectors.shape[0])
    cross_tile = lax.dot_general(
        all_vectors, rebuilt_t, (((0,), (1,)), ((), ())), preferred_element_type=jnp.float32
    ).astype(jnp.bfloat16)

    def apply_gram(rows_b, gram_b):
        return jnp.dot(
            rows_b,
            lax.all_gather(gram_b, "rot", axis=0, tiled=True),
            preferred_element_type=jnp.float32,
        )

    columns = cross_tile
    new_tile = None
    for iteration in range(ITERS):
        rows_b = lax.all_gather(columns, "dp", axis=1, tiled=True)
        gram_part = lax.psum_scatter(
            lax.dot_general(
                rows_b,
                columns,
                (((0,), (0,)), ((), ())),
                preferred_element_type=jnp.float32,
            ).astype(jnp.bfloat16),
            "rot",
            scatter_dimension=0,
            tiled=True,
        )
        if iteration == 0:
            gram_f = gram_part.astype(jnp.float32)
            total = lax.psum(jnp.sum(gram_f * gram_f), ("dp", "rot"))
            factor = 1.7 / jnp.sqrt(jnp.sqrt(total))
            product = apply_gram(rows_b, gram_part)
            new_tile = factor * (
                1.5 * columns.astype(jnp.float32) - 0.5 * (factor * factor) * product
            )
        else:
            product = apply_gram(rows_b, gram_part)
            new_tile = 1.5 * columns.astype(jnp.float32) - 0.5 * product
        columns = new_tile.astype(jnp.bfloat16)
    new_rotation = (math.sqrt(width) * new_tile).astype(jnp.bfloat16)
    return (codebook, new_rotation)


def solution(mesh):
    return jax.shard_map(
        body,
        mesh=mesh,
        in_specs=(P("dp", "rot"), P("rot", None), P("dp", "rot")),
        out_specs=(P("rot", None), P("rot", "dp")),
        check_vma=False,
    )
```

```python
import math

import jax
import jax.numpy as jnp
from jax import lax
from jax.sharding import PartitionSpec as P

K = 256
ITERS = 2


def body(vectors, rotation, codes):
    row_count, block_dims = vectors.shape
    width = rotation.shape[1]
    local_spaces = codes.shape[1]
    sub_dims = block_dims // local_spaces
    tile_cols = width // lax.axis_size("dp")
    tile_spaces = tile_cols // sub_dims
    dp_index = lax.axis_index("dp")
    code_ids = jnp.arange(K, dtype=jnp.int32)

    dp_size = lax.axis_size("dp")
    row_codes = lax.all_gather(codes, "rot", axis=1, tiled=True)

    def tile_part(block):
        block_codes = lax.dynamic_slice_in_dim(row_codes, block * tile_spaces, tile_spaces, 1)
        return jnp.concatenate([vectors, block_codes.astype(jnp.bfloat16)], axis=1)

    parts = [tile_part(dp_index)]
    for shift in range(1, dp_size):
        pairs = [(i, (i + shift) % dp_size) for i in range(dp_size)]
        parts.append(lax.ppermute(tile_part((dp_index + shift) % dp_size), "dp", pairs))
    joined = jnp.concatenate(parts, axis=0)
    all_vectors = joined[:, :block_dims]
    tile_codes = joined[:, block_dims:].astype(jnp.int32)

    rotated_t = lax.psum_scatter(
        lax.dot_general(
            rotation, vectors, (((0,), (1,)), ((), ())), preferred_element_type=jnp.float32
        ),
        "rot",
        scatter_dimension=0,
        tiled=True,
    ).astype(jnp.bfloat16)
    code_indicator = (codes.T[:, :, None] == code_ids[None, None, :]).astype(jnp.bfloat16)
    grouped_vectors = rotated_t.reshape(local_spaces, sub_dims, row_count)
    shard_code_sums = jnp.einsum(
        "vzo,voc->vzc", grouped_vectors, code_indicator, preferred_element_type=jnp.float32
    )
    local_counts = jnp.sum(code_indicator, axis=1, dtype=jnp.float32)
    total_sums, total_counts = lax.psum((shard_code_sums, local_counts), "dp")
    total_sums, total_counts, all_vectors, tile_codes = lax.optimization_barrier(
        (total_sums, total_counts, all_vectors, tile_codes)
    )
    book = total_sums / jnp.maximum(total_counts, 1.0)[:, None, :]
    codebook = book.reshape(block_dims, K)
    blocks_per_rot = local_spaces // tile_spaces
    offered = lax.dynamic_slice_in_dim(
        book.astype(jnp.bfloat16), (dp_index % blocks_per_rot) * tile_spaces, tile_spaces, 0
    )
    tile_book = lax.all_gather(offered, "rot", axis=0)[dp_index // blocks_per_rot]

    tile_indicator = (tile_codes.T[:, :, None] == code_ids[None, None, :]).astype(jnp.bfloat16)
    rebuilt_t = jnp.einsum(
        "lyg,lxg->lyx", tile_book, tile_indicator, preferred_element_type=jnp.float32
    )
    rebuilt_t = rebuilt_t.astype(jnp.bfloat16).reshape(tile_cols, all_vectors.shape[0])
    cross_tile = lax.dot_general(
        all_vectors, rebuilt_t, (((0,), (1,)), ((), ())), preferred_element_type=jnp.float32
    ).astype(jnp.bfloat16)

    def apply_gram(rows_b, gram_b):
        return jnp.dot(
            rows_b,
            lax.all_gather(gram_b, "rot", axis=0, tiled=True),
            preferred_element_type=jnp.float32,
        )

    columns = cross_tile
    new_tile = None
    for iteration in range(ITERS):
        rows_b = lax.all_gather(columns, "dp", axis=1, tiled=True)
        gram_part = lax.psum_scatter(
            lax.dot_general(
                rows_b,
                columns,
                (((0,), (0,)), ((), ())),
                preferred_element_type=jnp.float32,
            ).astype(jnp.bfloat16),
            "rot",
            scatter_dimension=0,
            tiled=True,
        )
        if iteration == 0:
            gram_f = gram_part.astype(jnp.float32)
            total = lax.psum(jnp.sum(gram_f * gram_f), ("dp", "rot"))
            factor = 1.7 / jnp.sqrt(jnp.sqrt(total))
            product = apply_gram(rows_b, gram_part)
            new_tile = factor * (
                1.5 * columns.astype(jnp.float32) - 0.5 * (factor * factor) * product
            )
        else:
            product = apply_gram(rows_b, gram_part)
            new_tile = 1.5 * columns.astype(jnp.float32) - 0.5 * product
        columns = new_tile.astype(jnp.bfloat16)
    new_rotation = (math.sqrt(width) * new_tile).astype(jnp.bfloat16)
    return (codebook, new_rotation)


def solution(mesh):
    return jax.shard_map(
        body,
        mesh=mesh,
        in_specs=(P("dp", "rot"), P("rot", None), P("dp", "rot")),
        out_specs=(P("rot", None), P("rot", "dp")),
        check_vma=False,
    )
```

```python
import math

import jax
import jax.numpy as jnp
from jax import lax
from jax.sharding import PartitionSpec as P

K = 256
ITERS = 2


def body(vectors, rotation, codes):
    row_count, block_dims = vectors.shape
    width = rotation.shape[1]
    local_spaces = codes.shape[1]
    sub_dims = block_dims // local_spaces
    tile_cols = width // lax.axis_size("dp")
    tile_spaces = tile_cols // sub_dims
    dp_index = lax.axis_index("dp")
    code_ids = jnp.arange(K, dtype=jnp.int32)

    dp_size = lax.axis_size("dp")
    row_codes = lax.all_gather(codes, "rot", axis=1, tiled=True)

    def tile_part(block):
        block_codes = lax.dynamic_slice_in_dim(row_codes, block * tile_spaces, tile_spaces, 1)
        return jnp.concatenate([vectors, block_codes.astype(jnp.bfloat16)], axis=1)

    parts = [tile_part(dp_index)]
    for shift in range(1, dp_size):
        pairs = [(i, (i + shift) % dp_size) for i in range(dp_size)]
        parts.append(lax.ppermute(tile_part((dp_index + shift) % dp_size), "dp", pairs))
    joined = jnp.concatenate(parts, axis=0)
    all_vectors = joined[:, :block_dims]
    tile_codes = joined[:, block_dims:].astype(jnp.int32)

    rotated_t = lax.psum_scatter(
        lax.dot_general(
            rotation, vectors, (((0,), (1,)), ((), ())), preferred_element_type=jnp.float32
        ),
        "rot",
        scatter_dimension=0,
        tiled=True,
    ).astype(jnp.bfloat16)
    code_indicator = (codes.T[:, :, None] == code_ids[None, None, :]).astype(jnp.bfloat16)
    grouped_vectors = rotated_t.reshape(local_spaces, sub_dims, row_count)
    shard_code_sums = jnp.einsum(
        "vzo,voc->vzc", grouped_vectors, code_indicator, preferred_element_type=jnp.float32
    )
    local_counts = jnp.sum(code_indicator, axis=1, dtype=jnp.float32)
    total_sums, total_counts = lax.psum((shard_code_sums, local_counts), "dp")
    total_sums, total_counts, all_vectors, tile_codes = lax.optimization_barrier(
        (total_sums, total_counts, all_vectors, tile_codes)
    )
    book = total_sums / jnp.maximum(total_counts, 1.0)[:, None, :]
    codebook = book.reshape(block_dims, K)
    blocks_per_rot = local_spaces // tile_spaces
    offered = lax.dynamic_slice_in_dim(
        book.astype(jnp.bfloat16), (dp_index % blocks_per_rot) * tile_spaces, tile_spaces, 0
    )
    tile_book = lax.all_gather(offered, "rot", axis=0)[dp_index // blocks_per_rot]

    tile_indicator = (tile_codes.T[:, :, None] == code_ids[None, None, :]).astype(jnp.bfloat16)
    rebuilt_t = jnp.einsum(
        "lyg,lxg->lyx", tile_book, tile_indicator, preferred_element_type=jnp.float32
    )
    rebuilt_t = rebuilt_t.astype(jnp.bfloat16).reshape(tile_cols, all_vectors.shape[0])
    cross_tile = lax.dot_general(
        all_vectors, rebuilt_t, (((0,), (1,)), ((), ())), preferred_element_type=jnp.float32
    ).astype(jnp.bfloat16)

    def apply_gram(rows_b, gram_b):
        return jnp.dot(
            rows_b,
            lax.all_gather(gram_b, "rot", axis=0, tiled=True),
            preferred_element_type=jnp.float32,
        )

    columns = cross_tile
    new_tile = None
    def row_panel(tile):
        if dp_size % 2:
            return lax.all_gather(tile, "dp", axis=1, tiled=True)
        groups = [list(range(parity, dp_size, 2)) for parity in range(2)]
        own = lax.all_gather(tile, "dp", axis=1, tiled=True, axis_index_groups=groups)
        mates = [(i, i ^ 1) for i in range(dp_size)]
        return jnp.concatenate([own, lax.ppermute(own, "dp", mates)], axis=1)

    for iteration in range(ITERS):
        rows_b = row_panel(columns)
        gram_part = lax.psum_scatter(
            lax.dot_general(
                rows_b,
                columns,
                (((0,), (0,)), ((), ())),
                preferred_element_type=jnp.float32,
            ).astype(jnp.bfloat16),
            "rot",
            scatter_dimension=0,
            tiled=True,
        )
        if iteration == 0:
            gram_f = gram_part.astype(jnp.float32)
            total = lax.psum(jnp.sum(gram_f * gram_f), ("dp", "rot"))
            factor = 1.7 / jnp.sqrt(jnp.sqrt(total))
            product = apply_gram(rows_b, gram_part)
            new_tile = factor * (
                1.5 * columns.astype(jnp.float32) - 0.5 * (factor * factor) * product
            )
        else:
            product = apply_gram(rows_b, gram_part)
            new_tile = 1.5 * columns.astype(jnp.float32) - 0.5 * product
        columns = new_tile.astype(jnp.bfloat16)
    new_rotation = (math.sqrt(width) * new_tile).astype(jnp.bfloat16)
    return (codebook, new_rotation)


def solution(mesh):
    return jax.shard_map(
        body,
        mesh=mesh,
        in_specs=(P("dp", "rot"), P("rot", None), P("dp", "rot")),
        out_specs=(P("rot", None), P("rot", "dp")),
        check_vma=False,
    )
```

```python
import math

import jax
import jax.numpy as jnp
from jax import lax
from jax.sharding import PartitionSpec as P

K = 256
ITERS = 2


def body(vectors, rotation, codes):
    row_count, block_dims = vectors.shape
    width = rotation.shape[1]
    local_spaces = codes.shape[1]
    sub_dims = block_dims // local_spaces
    tile_cols = width // lax.axis_size("dp")
    tile_spaces = tile_cols // sub_dims
    dp_index = lax.axis_index("dp")
    code_ids = jnp.arange(K, dtype=jnp.int32)

    dp_size = lax.axis_size("dp")
    row_codes = lax.all_gather(codes, "rot", axis=1, tiled=True)

    def block_codes(block):
        return lax.dynamic_slice_in_dim(
            row_codes, block * tile_spaces, tile_spaces, 1
        ).astype(jnp.bfloat16)

    if dp_size % 2:
        parts = [jnp.concatenate([vectors, block_codes(dp_index)], axis=1)]
        for shift in range(1, dp_size):
            pairs = [(i, (i + shift) % dp_size) for i in range(dp_size)]
            target = (dp_index + shift) % dp_size
            parts.append(
                lax.ppermute(jnp.concatenate([vectors, block_codes(target)], axis=1), "dp", pairs)
            )
        joined = jnp.concatenate(parts, axis=0)
    else:
        def pair_part(block):
            return jnp.concatenate(
                [vectors, block_codes(block), block_codes(block ^ 1)], axis=1
            )

        parts = [pair_part(dp_index)]
        for shift in range(2, dp_size, 2):
            pairs = [(i, (i + shift) % dp_size) for i in range(dp_size)]
            parts.append(lax.ppermute(pair_part((dp_index + shift) % dp_size), "dp", pairs))
        group = jnp.concatenate(parts, axis=0)
        mine = group[:, : block_dims + tile_spaces]
        for_mate = jnp.concatenate(
            [group[:, :block_dims], group[:, block_dims + tile_spaces :]], axis=1
        )
        mates = [(i, i ^ 1) for i in range(dp_size)]
        joined = jnp.concatenate([mine, lax.ppermute(for_mate, "dp", mates)], axis=0)
    all_vectors = joined[:, :block_dims]
    tile_codes = joined[:, block_dims:].astype(jnp.int32)

    rotated_t = lax.psum_scatter(
        lax.dot_general(
            rotation, vectors, (((0,), (1,)), ((), ())), preferred_element_type=jnp.float32
        ),
        "rot",
        scatter_dimension=0,
        tiled=True,
    ).astype(jnp.bfloat16)
    code_indicator = (codes.T[:, :, None] == code_ids[None, None, :]).astype(jnp.bfloat16)
    grouped_vectors = rotated_t.reshape(local_spaces, sub_dims, row_count)
    shard_code_sums = jnp.einsum(
        "vzo,voc->vzc", grouped_vectors, code_indicator, preferred_element_type=jnp.float32
    )
    local_counts = jnp.sum(code_indicator, axis=1, dtype=jnp.float32)
    total_sums, total_counts = lax.psum((shard_code_sums, local_counts), "dp")
    total_sums, total_counts, all_vectors, tile_codes = lax.optimization_barrier(
        (total_sums, total_counts, all_vectors, tile_codes)
    )
    book = total_sums / jnp.maximum(total_counts, 1.0)[:, None, :]
    codebook = book.reshape(block_dims, K)
    blocks_per_rot = local_spaces // tile_spaces
    offered = lax.dynamic_slice_in_dim(
        book.astype(jnp.bfloat16), (dp_index % blocks_per_rot) * tile_spaces, tile_spaces, 0
    )
    tile_book = lax.all_gather(offered, "rot", axis=0)[dp_index // blocks_per_rot]

    tile_indicator = (tile_codes.T[:, :, None] == code_ids[None, None, :]).astype(jnp.bfloat16)
    rebuilt_t = jnp.einsum(
        "lyg,lxg->lyx", tile_book, tile_indicator, preferred_element_type=jnp.float32
    )
    rebuilt_t = rebuilt_t.astype(jnp.bfloat16).reshape(tile_cols, all_vectors.shape[0])
    cross_tile = lax.dot_general(
        all_vectors, rebuilt_t, (((0,), (1,)), ((), ())), preferred_element_type=jnp.float32
    ).astype(jnp.bfloat16)

    def apply_gram(rows_b, gram_b):
        return jnp.dot(
            rows_b,
            lax.all_gather(gram_b, "rot", axis=0, tiled=True),
            preferred_element_type=jnp.float32,
        )

    columns = cross_tile
    new_tile = None
    for iteration in range(ITERS):
        rows_b = lax.all_gather(columns, "dp", axis=1, tiled=True)
        gram_part = lax.psum_scatter(
            lax.dot_general(
                rows_b,
                columns,
                (((0,), (0,)), ((), ())),
                preferred_element_type=jnp.float32,
            ).astype(jnp.bfloat16),
            "rot",
            scatter_dimension=0,
            tiled=True,
        )
        if iteration == 0:
            gram_f = gram_part.astype(jnp.float32)
            total = lax.psum(jnp.sum(gram_f * gram_f), ("dp", "rot"))
            factor = 1.7 / jnp.sqrt(jnp.sqrt(total))
            product = apply_gram(rows_b, gram_part)
            new_tile = factor * (
                1.5 * columns.astype(jnp.float32) - 0.5 * (factor * factor) * product
            )
        else:
            product = apply_gram(rows_b, gram_part)
            new_tile = 1.5 * columns.astype(jnp.float32) - 0.5 * product
        columns = new_tile.astype(jnp.bfloat16)
    new_rotation = (math.sqrt(width) * new_tile).astype(jnp.bfloat16)
    return (codebook, new_rotation)


def solution(mesh):
    return jax.shard_map(
        body,
        mesh=mesh,
        in_specs=(P("dp", "rot"), P("rot", None), P("dp", "rot")),
        out_specs=(P("rot", None), P("rot", "dp")),
        check_vma=False,
    )
```

```python
import math

import jax
import jax.numpy as jnp
from jax import lax
from jax.sharding import PartitionSpec as P

K = 256
ITERS = 2


def body(vectors, rotation, codes):
    row_count, block_dims = vectors.shape
    width = rotation.shape[1]
    local_spaces = codes.shape[1]
    sub_dims = block_dims // local_spaces
    tile_cols = width // lax.axis_size("dp")
    tile_spaces = tile_cols // sub_dims
    dp_index = lax.axis_index("dp")
    code_ids = jnp.arange(K, dtype=jnp.int32)

    dp_size = lax.axis_size("dp")
    row_codes = lax.all_gather(codes, "rot", axis=1, tiled=True)

    def block_codes(block):
        return lax.dynamic_slice_in_dim(
            row_codes, block * tile_spaces, tile_spaces, 1
        ).astype(jnp.bfloat16)

    if dp_size % 2:
        parts = [jnp.concatenate([vectors, block_codes(dp_index)], axis=1)]
        for shift in range(1, dp_size):
            pairs = [(i, (i + shift) % dp_size) for i in range(dp_size)]
            target = (dp_index + shift) % dp_size
            parts.append(
                lax.ppermute(jnp.concatenate([vectors, block_codes(target)], axis=1), "dp", pairs)
            )
        joined = jnp.concatenate(parts, axis=0)
    else:
        def pair_part(block):
            return jnp.concatenate(
                [vectors, block_codes(block), block_codes(block ^ 1)], axis=1
            )

        parts = [pair_part(dp_index)]
        for shift in range(2, dp_size, 2):
            pairs = [(i, (i + shift) % dp_size) for i in range(dp_size)]
            parts.append(lax.ppermute(pair_part((dp_index + shift) % dp_size), "dp", pairs))
        group = jnp.concatenate(parts, axis=0)
        mine = group[:, : block_dims + tile_spaces]
        for_mate = jnp.concatenate(
            [group[:, :block_dims], group[:, block_dims + tile_spaces :]], axis=1
        )
        mates = [(i, i ^ 1) for i in range(dp_size)]
        joined = jnp.concatenate([mine, lax.ppermute(for_mate, "dp", mates)], axis=0)
    all_vectors = joined[:, :block_dims]
    tile_codes = joined[:, block_dims:].astype(jnp.int32)

    rotated_t = lax.psum_scatter(
        lax.dot_general(
            rotation, vectors, (((0,), (1,)), ((), ())), preferred_element_type=jnp.float32
        ),
        "rot",
        scatter_dimension=0,
        tiled=True,
    ).astype(jnp.bfloat16)
    code_indicator = (codes.T[:, :, None] == code_ids[None, None, :]).astype(jnp.bfloat16)
    grouped_vectors = rotated_t.reshape(local_spaces, sub_dims, row_count)
    shard_code_sums = jnp.einsum(
        "vzo,voc->vzc", grouped_vectors, code_indicator, preferred_element_type=jnp.float32
    )
    local_counts = jnp.sum(code_indicator, axis=1, dtype=jnp.float32)
    total_sums, total_counts = lax.psum((shard_code_sums, local_counts), "dp")
    total_sums, total_counts, all_vectors, tile_codes = lax.optimization_barrier(
        (total_sums, total_counts, all_vectors, tile_codes)
    )
    book = total_sums / jnp.maximum(total_counts, 1.0)[:, None, :]
    codebook = book.reshape(block_dims, K)
    blocks_per_rot = local_spaces // tile_spaces
    offered = lax.dynamic_slice_in_dim(
        book.astype(jnp.bfloat16), (dp_index % blocks_per_rot) * tile_spaces, tile_spaces, 0
    )
    tile_book = lax.all_gather(offered, "rot", axis=0)[dp_index // blocks_per_rot]

    tile_indicator = (tile_codes.T[:, :, None] == code_ids[None, None, :]).astype(jnp.bfloat16)
    rebuilt_t = jnp.einsum(
        "lyg,lxg->lyx", tile_book, tile_indicator, preferred_element_type=jnp.float32
    )
    rebuilt_t = rebuilt_t.astype(jnp.bfloat16).reshape(tile_cols, all_vectors.shape[0])
    cross_tile = lax.dot_general(
        all_vectors, rebuilt_t, (((0,), (1,)), ((), ())), preferred_element_type=jnp.float32
    ).astype(jnp.bfloat16)

    def apply_gram(rows_b, gram_b):
        return jnp.dot(
            rows_b,
            lax.all_gather(gram_b, "rot", axis=0, tiled=True),
            preferred_element_type=jnp.float32,
        )

    columns = cross_tile
    new_tile = None
    for iteration in range(ITERS):
        rows_b = lax.all_gather(columns, "dp", axis=1, tiled=True)
        partial = lax.dot_general(
            rows_b,
            columns,
            (((0,), (0,)), ((), ())),
            preferred_element_type=jnp.float32,
        ).astype(jnp.bfloat16)
        if iteration == 0:
            gram_part = lax.psum_scatter(partial, "rot", scatter_dimension=0, tiled=True)
        else:
            gram_part = lax.psum(partial, "rot")
        if iteration == 0:
            gram_f = gram_part.astype(jnp.float32)
            total = lax.psum(jnp.sum(gram_f * gram_f), ("dp", "rot"))
            factor = 1.7 / jnp.sqrt(jnp.sqrt(total))
            product = apply_gram(rows_b, gram_part)
            new_tile = factor * (
                1.5 * columns.astype(jnp.float32) - 0.5 * (factor * factor) * product
            )
        else:
            product = jnp.dot(rows_b, gram_part, preferred_element_type=jnp.float32)
            new_tile = 1.5 * columns.astype(jnp.float32) - 0.5 * product
        columns = new_tile.astype(jnp.bfloat16)
    new_rotation = (math.sqrt(width) * new_tile).astype(jnp.bfloat16)
    return (codebook, new_rotation)


def solution(mesh):
    return jax.shard_map(
        body,
        mesh=mesh,
        in_specs=(P("dp", "rot"), P("rot", None), P("dp", "rot")),
        out_specs=(P("rot", None), P("rot", "dp")),
        check_vma=False,
    )
```

```python
import math

import jax
import jax.numpy as jnp
from jax import lax
from jax.sharding import PartitionSpec as P

K = 256
ITERS = 2


def body(vectors, rotation, codes):
    row_count, block_dims = vectors.shape
    width = rotation.shape[1]
    local_spaces = codes.shape[1]
    sub_dims = block_dims // local_spaces
    tile_cols = width // lax.axis_size("dp")
    tile_spaces = tile_cols // sub_dims
    dp_index = lax.axis_index("dp")
    code_ids = jnp.arange(K, dtype=jnp.int32)

    dp_size = lax.axis_size("dp")
    row_codes = lax.all_gather(codes, "rot", axis=1, tiled=True)

    def block_codes(block):
        return lax.dynamic_slice_in_dim(
            row_codes, block * tile_spaces, tile_spaces, 1
        ).astype(jnp.bfloat16)

    if dp_size % 2:
        parts = [jnp.concatenate([vectors, block_codes(dp_index)], axis=1)]
        for shift in range(1, dp_size):
            pairs = [(i, (i + shift) % dp_size) for i in range(dp_size)]
            target = (dp_index + shift) % dp_size
            parts.append(
                lax.ppermute(jnp.concatenate([vectors, block_codes(target)], axis=1), "dp", pairs)
            )
        joined = jnp.concatenate(parts, axis=0)
    else:
        def pair_part(block):
            return jnp.concatenate(
                [vectors, block_codes(block), block_codes(block ^ 1)], axis=1
            )

        parts = [pair_part(dp_index)]
        for shift in range(2, dp_size, 2):
            pairs = [(i, (i + shift) % dp_size) for i in range(dp_size)]
            parts.append(lax.ppermute(pair_part((dp_index + shift) % dp_size), "dp", pairs))
        group = jnp.concatenate(parts, axis=0)
        mine = group[:, : block_dims + tile_spaces]
        for_mate = jnp.concatenate(
            [group[:, :block_dims], group[:, block_dims + tile_spaces :]], axis=1
        )
        mates = [(i, i ^ 1) for i in range(dp_size)]
        joined = jnp.concatenate([mine, lax.ppermute(for_mate, "dp", mates)], axis=0)
    all_vectors = joined[:, :block_dims]
    tile_codes = joined[:, block_dims:].astype(jnp.int32)

    rotated_t = lax.psum_scatter(
        lax.dot_general(
            rotation, vectors, (((0,), (1,)), ((), ())), preferred_element_type=jnp.float32
        ),
        "rot",
        scatter_dimension=0,
        tiled=True,
    ).astype(jnp.bfloat16)
    code_indicator = (codes.T[:, :, None] == code_ids[None, None, :]).astype(jnp.bfloat16)
    grouped_vectors = rotated_t.reshape(local_spaces, sub_dims, row_count)
    shard_code_sums = jnp.einsum(
        "vzo,voc->vzc", grouped_vectors, code_indicator, preferred_element_type=jnp.float32
    )
    local_counts = jnp.sum(code_indicator, axis=1, dtype=jnp.float32)
    total_sums, total_counts = lax.psum((shard_code_sums, local_counts), "dp")
    book = total_sums / jnp.maximum(total_counts, 1.0)[:, None, :]
    codebook = book.reshape(block_dims, K)
    blocks_per_rot = local_spaces // tile_spaces
    offered = lax.dynamic_slice_in_dim(
        book.astype(jnp.bfloat16), (dp_index % blocks_per_rot) * tile_spaces, tile_spaces, 0
    )
    tile_book = lax.all_gather(offered, "rot", axis=0)[dp_index // blocks_per_rot]
    tile_book, all_vectors, tile_codes = lax.optimization_barrier(
        (tile_book, all_vectors, tile_codes)
    )

    tile_indicator = (tile_codes.T[:, :, None] == code_ids[None, None, :]).astype(jnp.bfloat16)
    rebuilt_t = jnp.einsum(
        "lyg,lxg->lyx", tile_book, tile_indicator, preferred_element_type=jnp.float32
    )
    rebuilt_t = rebuilt_t.astype(jnp.bfloat16).reshape(tile_cols, all_vectors.shape[0])
    cross_tile = lax.dot_general(
        all_vectors, rebuilt_t, (((0,), (1,)), ((), ())), preferred_element_type=jnp.float32
    ).astype(jnp.bfloat16)

    def apply_gram(rows_b, gram_b):
        return jnp.dot(
            rows_b,
            lax.all_gather(gram_b, "rot", axis=0, tiled=True),
            preferred_element_type=jnp.float32,
        )

    columns = cross_tile
    new_tile = None
    for iteration in range(ITERS):
        rows_b = lax.all_gather(columns, "dp", axis=1, tiled=True)
        partial = lax.dot_general(
            rows_b,
            columns,
            (((0,), (0,)), ((), ())),
            preferred_element_type=jnp.float32,
        ).astype(jnp.bfloat16)
        if iteration == 0:
            gram_part = lax.psum_scatter(partial, "rot", scatter_dimension=0, tiled=True)
        else:
            gram_part = lax.psum(partial, "rot")
        if iteration == 0:
            gram_f = gram_part.astype(jnp.float32)
            total = lax.psum(jnp.sum(gram_f * gram_f), ("dp", "rot"))
            factor = 1.7 / jnp.sqrt(jnp.sqrt(total))
            product = apply_gram(rows_b, gram_part)
            new_tile = factor * (
                1.5 * columns.astype(jnp.float32) - 0.5 * (factor * factor) * product
            )
        else:
            product = jnp.dot(rows_b, gram_part, preferred_element_type=jnp.float32)
            new_tile = 1.5 * columns.astype(jnp.float32) - 0.5 * product
        columns = new_tile.astype(jnp.bfloat16)
    new_rotation = (math.sqrt(width) * new_tile).astype(jnp.bfloat16)
    return (codebook, new_rotation)


def solution(mesh):
    return jax.shard_map(
        body,
        mesh=mesh,
        in_specs=(P("dp", "rot"), P("rot", None), P("dp", "rot")),
        out_specs=(P("rot", None), P("rot", "dp")),
        check_vma=False,
    )
```

```python
import math

import jax
import jax.numpy as jnp
from jax import lax
from jax.sharding import PartitionSpec as P

K = 256
ITERS = 2


def body(vectors, rotation, codes):
    row_count, block_dims = vectors.shape
    width = rotation.shape[1]
    local_spaces = codes.shape[1]
    sub_dims = block_dims // local_spaces
    tile_cols = width // lax.axis_size("dp")
    tile_spaces = tile_cols // sub_dims
    dp_index = lax.axis_index("dp")
    code_ids = jnp.arange(K, dtype=jnp.int32)

    dp_size = lax.axis_size("dp")
    row_codes = lax.all_gather(codes, "rot", axis=1, tiled=True)

    def block_codes(block):
        return lax.dynamic_slice_in_dim(
            row_codes, block * tile_spaces, tile_spaces, 1
        ).astype(jnp.bfloat16)

    if dp_size % 2:
        parts = [jnp.concatenate([vectors, block_codes(dp_index)], axis=1)]
        for shift in range(1, dp_size):
            pairs = [(i, (i + shift) % dp_size) for i in range(dp_size)]
            target = (dp_index + shift) % dp_size
            parts.append(
                lax.ppermute(jnp.concatenate([vectors, block_codes(target)], axis=1), "dp", pairs)
            )
        joined = jnp.concatenate(parts, axis=0)
    else:
        def pair_part(block):
            return jnp.concatenate(
                [vectors, block_codes(block), block_codes(block ^ 1)], axis=1
            )

        parts = [pair_part(dp_index)]
        for shift in range(2, dp_size, 2):
            pairs = [(i, (i + shift) % dp_size) for i in range(dp_size)]
            parts.append(lax.ppermute(pair_part((dp_index + shift) % dp_size), "dp", pairs))
        group = jnp.concatenate(parts, axis=0)
        mine = group[:, : block_dims + tile_spaces]
        for_mate = jnp.concatenate(
            [group[:, :block_dims], group[:, block_dims + tile_spaces :]], axis=1
        )
        mates = [(i, i ^ 1) for i in range(dp_size)]
        joined = jnp.concatenate([mine, lax.ppermute(for_mate, "dp", mates)], axis=0)
    all_vectors = joined[:, :block_dims]
    tile_codes = joined[:, block_dims:].astype(jnp.int32)

    rotated_t = lax.psum_scatter(
        lax.dot_general(
            rotation, vectors, (((0,), (1,)), ((), ())), preferred_element_type=jnp.float32
        ),
        "rot",
        scatter_dimension=0,
        tiled=True,
    ).astype(jnp.bfloat16)
    code_indicator = (codes.T[:, :, None] == code_ids[None, None, :]).astype(jnp.bfloat16)
    grouped_vectors = rotated_t.reshape(local_spaces, sub_dims, row_count)
    shard_code_sums = jnp.einsum(
        "vzo,voc->vzc", grouped_vectors, code_indicator, preferred_element_type=jnp.float32
    )
    local_counts = jnp.sum(code_indicator, axis=1, dtype=jnp.float32)
    total_sums, total_counts = lax.psum((shard_code_sums, local_counts), "dp")
    book = total_sums / jnp.maximum(total_counts, 1.0)[:, None, :]
    codebook = book.reshape(block_dims, K)
    blocks_per_rot = local_spaces // tile_spaces
    offered = lax.dynamic_slice_in_dim(
        book.astype(jnp.bfloat16), (dp_index % blocks_per_rot) * tile_spaces, tile_spaces, 0
    )
    tile_book = lax.all_gather(offered, "rot", axis=0)[dp_index // blocks_per_rot]
    tile_book, all_vectors, tile_codes = lax.optimization_barrier(
        (tile_book, all_vectors, tile_codes)
    )

    rebuilt_t = jnp.take_along_axis(tile_book, tile_codes.T[:, None, :], axis=2)
    rebuilt_t = rebuilt_t.astype(jnp.bfloat16).reshape(tile_cols, all_vectors.shape[0])
    cross_tile = lax.dot_general(
        all_vectors, rebuilt_t, (((0,), (1,)), ((), ())), preferred_element_type=jnp.float32
    ).astype(jnp.bfloat16)

    def apply_gram(rows_b, gram_b):
        return jnp.dot(
            rows_b,
            lax.all_gather(gram_b, "rot", axis=0, tiled=True),
            preferred_element_type=jnp.float32,
        )

    columns = cross_tile
    new_tile = None
    for iteration in range(ITERS):
        rows_b = lax.all_gather(columns, "dp", axis=1, tiled=True)
        partial = lax.dot_general(
            rows_b,
            columns,
            (((0,), (0,)), ((), ())),
            preferred_element_type=jnp.float32,
        ).astype(jnp.bfloat16)
        if iteration == 0:
            gram_part = lax.psum_scatter(partial, "rot", scatter_dimension=0, tiled=True)
        else:
            gram_part = lax.psum(partial, "rot")
        if iteration == 0:
            gram_f = gram_part.astype(jnp.float32)
            total = lax.psum(jnp.sum(gram_f * gram_f), ("dp", "rot"))
            factor = 1.7 / jnp.sqrt(jnp.sqrt(total))
            product = apply_gram(rows_b, gram_part)
            new_tile = factor * (
                1.5 * columns.astype(jnp.float32) - 0.5 * (factor * factor) * product
            )
        else:
            product = jnp.dot(rows_b, gram_part, preferred_element_type=jnp.float32)
            new_tile = 1.5 * columns.astype(jnp.float32) - 0.5 * product
        columns = new_tile.astype(jnp.bfloat16)
    new_rotation = (math.sqrt(width) * new_tile).astype(jnp.bfloat16)
    return (codebook, new_rotation)


def solution(mesh):
    return jax.shard_map(
        body,
        mesh=mesh,
        in_specs=(P("dp", "rot"), P("rot", None), P("dp", "rot")),
        out_specs=(P("rot", None), P("rot", "dp")),
        check_vma=False,
    )
```

```python
import math

import jax
import jax.numpy as jnp
from jax import lax
from jax.sharding import PartitionSpec as P

K = 256
ITERS = 2


def body(vectors, rotation, codes):
    row_count, block_dims = vectors.shape
    width = rotation.shape[1]
    local_spaces = codes.shape[1]
    sub_dims = block_dims // local_spaces
    tile_cols = width // lax.axis_size("dp")
    tile_spaces = tile_cols // sub_dims
    dp_index = lax.axis_index("dp")
    code_ids = jnp.arange(K, dtype=jnp.int32)

    dp_size = lax.axis_size("dp")
    row_codes = lax.all_gather(codes, "rot", axis=1, tiled=True)

    def block_codes(block):
        return lax.dynamic_slice_in_dim(
            row_codes, block * tile_spaces, tile_spaces, 1
        ).astype(jnp.bfloat16)

    if dp_size % 2:
        parts = [jnp.concatenate([vectors, block_codes(dp_index)], axis=1)]
        for shift in range(1, dp_size):
            pairs = [(i, (i + shift) % dp_size) for i in range(dp_size)]
            target = (dp_index + shift) % dp_size
            parts.append(
                lax.ppermute(jnp.concatenate([vectors, block_codes(target)], axis=1), "dp", pairs)
            )
        joined = jnp.concatenate(parts, axis=0)
    else:
        def pair_part(block):
            return jnp.concatenate(
                [vectors, block_codes(block), block_codes(block ^ 1)], axis=1
            )

        parts = [pair_part(dp_index)]
        for shift in range(2, dp_size, 2):
            pairs = [(i, (i + shift) % dp_size) for i in range(dp_size)]
            parts.append(lax.ppermute(pair_part((dp_index + shift) % dp_size), "dp", pairs))
        group = jnp.concatenate(parts, axis=0)
        mine = group[:, : block_dims + tile_spaces]
        for_mate = jnp.concatenate(
            [group[:, :block_dims], group[:, block_dims + tile_spaces :]], axis=1
        )
        mates = [(i, i ^ 1) for i in range(dp_size)]
        joined = jnp.concatenate([mine, lax.ppermute(for_mate, "dp", mates)], axis=0)
    all_vectors = joined[:, :block_dims]
    tile_codes = joined[:, block_dims:].astype(jnp.int32)

    rotated_t = lax.psum_scatter(
        lax.dot_general(
            rotation, vectors, (((0,), (1,)), ((), ())), preferred_element_type=jnp.float32
        ),
        "rot",
        scatter_dimension=0,
        tiled=True,
    ).astype(jnp.bfloat16)
    code_indicator = (codes.T[:, :, None] == code_ids[None, None, :]).astype(jnp.bfloat16)
    grouped_vectors = rotated_t.reshape(local_spaces, sub_dims, row_count)
    shard_code_sums = jnp.einsum(
        "vzo,voc->vzc", grouped_vectors, code_indicator, preferred_element_type=jnp.float32
    )
    local_counts = jnp.sum(code_indicator, axis=1, dtype=jnp.float32)
    total_sums, total_counts = lax.psum((shard_code_sums, local_counts), "dp")
    book = total_sums / jnp.maximum(total_counts, 1.0)[:, None, :]
    codebook = book.reshape(block_dims, K)
    blocks_per_rot = local_spaces // tile_spaces
    offered = lax.dynamic_slice_in_dim(
        book.astype(jnp.bfloat16), (dp_index % blocks_per_rot) * tile_spaces, tile_spaces, 0
    )
    tile_book = lax.all_gather(offered, "rot", axis=0)[dp_index // blocks_per_rot]
    tile_book, all_vectors, tile_codes = lax.optimization_barrier(
        (tile_book, all_vectors, tile_codes)
    )

    tile_indicator = (tile_codes.T[:, :, None] == code_ids[None, None, :]).astype(jnp.bfloat16)
    rebuilt = jnp.einsum(
        "lxg,lyg->lxy", tile_indicator, tile_book, preferred_element_type=jnp.float32
    ).astype(jnp.bfloat16)
    cross_tile = jnp.einsum(
        "xa,lxy->aly", all_vectors, rebuilt, preferred_element_type=jnp.float32
    ).reshape(block_dims, tile_cols).astype(jnp.bfloat16)

    def apply_gram(rows_b, gram_b):
        return jnp.dot(
            rows_b,
            lax.all_gather(gram_b, "rot", axis=0, tiled=True),
            preferred_element_type=jnp.float32,
        )

    columns = cross_tile
    new_tile = None
    for iteration in range(ITERS):
        rows_b = lax.all_gather(columns, "dp", axis=1, tiled=True)
        partial = lax.dot_general(
            rows_b,
            columns,
            (((0,), (0,)), ((), ())),
            preferred_element_type=jnp.float32,
        ).astype(jnp.bfloat16)
        if iteration == 0:
            gram_part = lax.psum_scatter(partial, "rot", scatter_dimension=0, tiled=True)
        else:
            gram_part = lax.psum(partial, "rot")
        if iteration == 0:
            gram_f = gram_part.astype(jnp.float32)
            total = lax.psum(jnp.sum(gram_f * gram_f), ("dp", "rot"))
            factor = 1.7 / jnp.sqrt(jnp.sqrt(total))
            product = apply_gram(rows_b, gram_part)
            new_tile = factor * (
                1.5 * columns.astype(jnp.float32) - 0.5 * (factor * factor) * product
            )
        else:
            product = jnp.dot(rows_b, gram_part, preferred_element_type=jnp.float32)
            new_tile = 1.5 * columns.astype(jnp.float32) - 0.5 * product
        columns = new_tile.astype(jnp.bfloat16)
    new_rotation = (math.sqrt(width) * new_tile).astype(jnp.bfloat16)
    return (codebook, new_rotation)


def solution(mesh):
    return jax.shard_map(
        body,
        mesh=mesh,
        in_specs=(P("dp", "rot"), P("rot", None), P("dp", "rot")),
        out_specs=(P("rot", None), P("rot", "dp")),
        check_vma=False,
    )
```
